256 devices in a mesh: blk: 16 (over z_hi, y), head: 16 (over z_lo, x, core).
Axes of the slice: x: 4, y: 4, z: 8 (z_hi: 4, z_lo: 2; z = z_hi * 2 + z_lo), core: 2. Of those that a mesh axis runs over, the one named last changes fastest.
Arguments:
- query_heads: bfloat16 [3072, 24576], P('blk', 'head'), may hold values from -200 to 200
- latent_cache: bfloat16 [3072, 512], P('blk'), may hold values from -6 to 6
- rope_keys: bfloat16 [3072, 64], P('blk'), may hold values from -10 to 10
- up_weight: bfloat16 [512, 32768], P('blk', 'head'), may hold values from -0.25 to 0.25
- out_weight: bfloat16 [16384, 5120], P('head'), may hold values from -0.046875 to 0.046875
- block_mask: int32 [32, 32], replicated, may hold values from 0 to 1, as said below
Outputs:
- attended: bfloat16 [3072, 5120], P('blk', 'head')
The draws below stay inside these ranges and needn't reach their ends.
Inputs may be any that keep to these rules, and one draw needn't show every extreme that they name: block_mask[i, i] is 1 and block_mask[i, j] is 0 for j > i; entries below the diagonal are 0 or 1.
All inputs are finite; a program needn't handle non-finite values.
Results may differ from the reference program's by a relative error of at most 0.019.
Values may be sent and summed in bfloat16 or wider, within the bound.
No kernel may reach another device: no remote copies, remote signals or barrier semaphores. Data moves between devices by JAX's collectives and lax.ppermute only.
A program may use at most 64 MiB of HBM per device.

```python
import math
import jax
import jax.numpy as jnp
from jax import lax

D = 5120
H = 128
DN = 128
DR = 64
DV = 128
KVR = 512
QB = 96
TOKENS = 3072
NBLK = 32
N_HEAD = 16


def draw_query_heads(key, part):
    shape = (TOKENS, H, DN + DR)
    base_draw = jnp.clip(jax.random.normal(jax.random.fold_in(key, 1), shape, jnp.float32), -6.0, 6.0)
    return base_draw.reshape(TOKENS, H * (DN + DR)).astype(jnp.bfloat16)


def draw_rope_keys(key, part):
    shape = (TOKENS, DR)
    base_draw = jnp.clip(jax.random.normal(jax.random.fold_in(key, 2), shape, jnp.float32), -6.0, 6.0)
    return base_draw.astype(jnp.bfloat16)


def draw_block_mask(key, part):
    random_bits = jax.random.randint(jax.random.fold_in(key, 3), (NBLK, NBLK), 0, 2)
    row_index = jnp.arange(NBLK)[:, None]
    column_index = jnp.arange(NBLK)[None, :]
    kept = jnp.where(column_index == row_index, 1, jnp.where(column_index < row_index, random_bits, 0))
    return kept.astype(jnp.int32)


def level_of(rng, shape, cuts, least, top_value):
    def one(axis_at, shards_of):
        steps = jax.random.uniform(jax.random.fold_in(jax.random.fold_in(rng, 6), axis_at), (shards_of,), jnp.float32, least / len(cuts), top_value / len(cuts))
        return jnp.repeat(jnp.exp(steps), shape[axis_at] // shards_of).reshape((-1,) + (1,) * (len(shape) - axis_at - 1))

    level = one(*cuts[0])
    for cut in cuts[1:]:
        level = level * one(*cut)
    return level


def bell_draw(own_key, shape, spread, reach, pieces=(), kind=jnp.bfloat16):
    loudness = level_of(own_key, shape, pieces, -0.22, 0.18) if pieces else 1.0
    values = jax.random.normal(own_key, shape, jnp.float32) * spread * loudness
    return jnp.minimum(jnp.maximum(values, -reach), reach).astype(kind)


def setup_inputs(seed: int = 0) -> dict:
    arg_keys = jax.random.split(jax.random.key(seed), 7)
    return {
        "query_heads": draw_query_heads(jax.random.fold_in(arg_keys[6], 71), 0),
        "latent_cache": bell_draw(arg_keys[1], (TOKENS, KVR), 1.0, 6.0, ((0, 16),)),
        "rope_keys": draw_rope_keys(jax.random.fold_in(arg_keys[6], 71), 0),
        "up_weight": bell_draw(arg_keys[3], (KVR, H * (DN + DV)), KVR ** -0.5, 0.25, ((0, 16), (1, 16))),
        "out_weight": bell_draw(arg_keys[4], (H * DV, D), (H * DV) ** -0.5, 0.046875, ((0, 16),)),
        "block_mask": draw_block_mask(jax.random.fold_in(arg_keys[6], 71), 0),
    }


NEG_FILL = -1e+30

def reference(query_heads, latent_cache, rope_keys, up_weight, out_weight, block_mask):
    token_count = query_heads.shape[0]
    queries = query_heads.reshape(token_count, H, DN + DR)
    expanded = jnp.dot(latent_cache, up_weight, preferred_element_type=jnp.float32).astype(jnp.bfloat16)
    expanded = expanded.reshape(token_count, H, DN + DV)
    position = jnp.arange(token_count, dtype=jnp.int32)
    block_id = position // QB
    block_rows = jnp.take(block_mask, block_id, axis=0)
    block_bits = jnp.take(block_rows, block_id, axis=1)
    allowed = (block_bits == 1) & (position[None, :] <= position[:, None])
    score_scale = 1.0 / math.sqrt(DN + DR)

    def one_head(operands):
        query_part, key_value = operands
        scores = jnp.dot(query_part[:, :DN], key_value[:, :DN].T, preferred_element_type=jnp.float32)
        scores = scores + jnp.dot(query_part[:, DN:], rope_keys.T, preferred_element_type=jnp.float32)
        scores = jnp.where(allowed, scores * score_scale, NEG_FILL)
        row_max = lax.optimization_barrier(jnp.max(scores, axis=1, keepdims=True))
        weights = jnp.where(allowed, jnp.exp(scores - row_max), 0.0)
        denominator = lax.optimization_barrier(jnp.sum(weights, axis=1, keepdims=True))
        mixed = jnp.dot(weights.astype(jnp.bfloat16), key_value[:, DN:], preferred_element_type=jnp.float32)
        return (mixed / denominator).astype(jnp.bfloat16)
    per_head = lax.map(one_head, (jnp.transpose(queries, (1, 0, 2)), jnp.transpose(expanded, (1, 0, 2))))
    group_width = H // N_HEAD * DV
    outputs = jnp.transpose(per_head, (1, 0, 2)).reshape(token_count, N_HEAD, group_width)
    outputs = jnp.transpose(outputs, (1, 0, 2))
    weight_groups = out_weight.reshape(N_HEAD, group_width, D)

    def add_group(running_sum, operands):
        partial_sum = jnp.dot(operands[0], operands[1], preferred_element_type=jnp.float32).astype(jnp.bfloat16)
        partial_sum = lax.optimization_barrier(partial_sum)
        return (running_sum + partial_sum.astype(jnp.float32), None)
    summed_out, unused = lax.scan(add_group, jnp.zeros((token_count, D), jnp.float32), (outputs, weight_groups))
    return summed_out.astype(jnp.bfloat16)
```

```python
import math

import jax
import jax.numpy as jnp
from jax import lax
from jax.sharding import PartitionSpec as P

DN = 128
DR = 64
DV = 128
QB = 96


NEG_FILL = -1e30


def per_device(query_heads, latent_cache, rope_keys, up_weight, out_weight, block_mask):
    tok_rows = query_heads.shape[0]
    head_count = out_weight.shape[0] // DV
    blk_count = lax.axis_size("blk")
    head_devs = lax.axis_size("head")
    my_index = lax.axis_index("blk")
    all_tokens = tok_rows * blk_count
    queries = query_heads.reshape(tok_rows, head_count, DN + DR)
    query_nope = queries[:, :, :DN]
    query_rot = queries[:, :, DN:]
    score_scale = 1.0 / math.sqrt(DN + DR)

    payload = jnp.concatenate([latent_cache, rope_keys], axis=1)
    payload_all = lax.all_gather(payload, "blk", axis=0, tiled=True)
    latent_all = payload_all[:, : latent_cache.shape[1]]
    rope_all = payload_all[:, latent_cache.shape[1]:]

    spread = jnp.broadcast_to(up_weight[None], (blk_count,) + up_weight.shape)
    full_up = lax.all_to_all(spread, "blk", 0, 0, tiled=False).reshape(-1, up_weight.shape[1])

    expanded = jnp.dot(latent_all, full_up, preferred_element_type=jnp.float32).astype(jnp.bfloat16)
    expanded = expanded.reshape(all_tokens, head_count, DN + DV)

    query_pos = my_index * tok_rows + jnp.arange(tok_rows, dtype=jnp.int32)
    key_pos = jnp.arange(all_tokens, dtype=jnp.int32)
    mask_rows = lax.dynamic_slice_in_dim(block_mask, my_index * (tok_rows // QB), tok_rows // QB, 0)
    bits = jnp.repeat(jnp.repeat(mask_rows, QB, axis=0), QB, axis=1) == 1
    allowed = bits & (key_pos[None, :] <= query_pos[:, None])

    scores = jnp.einsum(
        "qhd,khd->hqk", query_nope, expanded[:, :, :DN], preferred_element_type=jnp.float32
    )
    scores = scores + jnp.einsum(
        "qhr,kr->hqk", query_rot, rope_all, preferred_element_type=jnp.float32
    )
    scores = jnp.where(allowed[None], scores * score_scale, NEG_FILL)
    row_max = jnp.max(scores, axis=2, keepdims=True)
    weights = jnp.where(allowed[None], jnp.exp(scores - row_max), 0.0)
    denominator = jnp.sum(weights, axis=2)
    mixed = jnp.einsum(
        "hqk,khv->hqv",
        weights.astype(jnp.bfloat16),
        expanded[:, :, DN:],
        preferred_element_type=jnp.float32,
    )
    outputs = (mixed / denominator[:, :, None]).astype(jnp.bfloat16)
    outputs = jnp.transpose(outputs, (1, 0, 2)).reshape(tok_rows, head_count * DV)
    partial_sum = jnp.dot(outputs, out_weight, preferred_element_type=jnp.float32).astype(jnp.bfloat16)

    pieces = partial_sum.reshape(tok_rows, head_devs, -1)
    pieces = lax.all_to_all(pieces, "head", 1, 1, tiled=False)
    return pieces.astype(jnp.float32).sum(axis=1).astype(jnp.bfloat16)


def solution(mesh):
    return jax.shard_map(
        per_device,
        mesh=mesh,
        in_specs=(
            P("blk", "head"),
            P("blk", None),
            P("blk", None),
            P("blk", "head"),
            P("head", None),
            P(),
        ),
        out_specs=P("blk", "head"),
        check_vma=False,
    )
```

```python
import math

import jax
import jax.numpy as jnp
import numpy as np
from jax import lax
from jax.sharding import Mesh, PartitionSpec as P

DN = 128
DR = 64
DV = 128
QB = 96


NEG_FILL = -1e30
HEAD = ("hh", "hc")


def swap_cores(value):
    return lax.ppermute(value, "hc", [(0, 1), (1, 0)])


def per_device(query_heads, latent_cache, rope_keys, up_weight, out_weight, block_mask):
    tok_rows = query_heads.shape[0]
    head_count = out_weight.shape[0] // DV
    blk_count = lax.axis_size("blk")
    chips = lax.axis_size("hh")
    my_index = lax.axis_index("blk")
    core = lax.axis_index("hc")
    all_tokens = tok_rows * blk_count
    queries = query_heads.reshape(tok_rows, head_count, DN + DR)
    query_nope = queries[:, :, :DN]
    query_rot = queries[:, :, DN:]
    score_scale = 1.0 / math.sqrt(DN + DR)

    payload = jnp.concatenate([latent_cache, rope_keys], axis=1)
    width = payload.shape[1] // 2
    mine = lax.dynamic_slice_in_dim(payload, core * width, width, 1)
    mine_all = lax.all_gather(mine, "blk", axis=0, tiled=True)
    theirs_all = swap_cores(mine_all)
    doubled = jnp.concatenate([mine_all, theirs_all, mine_all], axis=1)
    payload_all = lax.dynamic_slice_in_dim(doubled, core * width, 2 * width, 1)
    latent_all = payload_all[:, : latent_cache.shape[1]]
    rope_all = payload_all[:, latent_cache.shape[1]:]

    spread = jnp.broadcast_to(up_weight[None], (blk_count,) + up_weight.shape)
    full_up = lax.all_to_all(spread, "blk", 0, 0, tiled=False).reshape(-1, up_weight.shape[1])

    expanded = jnp.dot(latent_all, full_up, preferred_element_type=jnp.float32).astype(jnp.bfloat16)
    expanded = expanded.reshape(all_tokens, head_count, DN + DV)

    query_pos = my_index * tok_rows + jnp.arange(tok_rows, dtype=jnp.int32)
    key_pos = jnp.arange(all_tokens, dtype=jnp.int32)
    mask_rows = lax.dynamic_slice_in_dim(block_mask, my_index * (tok_rows // QB), tok_rows // QB, 0)
    bits = jnp.repeat(jnp.repeat(mask_rows, QB, axis=0), QB, axis=1) == 1
    allowed = bits & (key_pos[None, :] <= query_pos[:, None])

    scores = jnp.einsum(
        "qhd,khd->hqk", query_nope, expanded[:, :, :DN], preferred_element_type=jnp.float32
    )
    scores = scores + jnp.einsum(
        "qhr,kr->hqk", query_rot, rope_all, preferred_element_type=jnp.float32
    )
    scores = jnp.where(allowed[None], scores * score_scale, NEG_FILL)
    row_max = jnp.max(scores, axis=2, keepdims=True)
    weights = jnp.where(allowed[None], jnp.exp(scores - row_max), 0.0)
    denominator = jnp.sum(weights, axis=2)
    mixed = jnp.einsum(
        "hqk,khv->hqv",
        weights.astype(jnp.bfloat16),
        expanded[:, :, DN:],
        preferred_element_type=jnp.float32,
    )
    outputs = (mixed / denominator[:, :, None]).astype(jnp.bfloat16)
    outputs = jnp.transpose(outputs, (1, 0, 2)).reshape(tok_rows, head_count * DV)
    partial_sum = jnp.dot(outputs, out_weight, preferred_element_type=jnp.float32).astype(jnp.bfloat16)

    pieces = partial_sum.reshape(tok_rows, chips, 2, -1)
    keep = lax.dynamic_index_in_dim(pieces, core, 2, keepdims=False)
    give = lax.dynamic_index_in_dim(pieces, 1 - core, 2, keepdims=False)
    paired = (keep.astype(jnp.float32) + swap_cores(give).astype(jnp.float32)).astype(jnp.bfloat16)
    paired = lax.all_to_all(paired, "hh", 1, 1, tiled=False)
    return paired.astype(jnp.float32).sum(axis=1).astype(jnp.bfloat16)


def solution(mesh):
    blk, heads = mesh.devices.shape
    split = Mesh(np.asarray(mesh.devices).reshape(blk, heads // 2, 2), ("blk",) + HEAD)
    return jax.shard_map(
        per_device,
        mesh=split,
        in_specs=(
            P("blk", HEAD),
            P("blk", None),
            P("blk", None),
            P("blk", HEAD),
            P(HEAD, None),
            P(),
        ),
        out_specs=P("blk", HEAD),
        check_vma=False,
    )
```

```python
import math

import jax
import jax.numpy as jnp
import numpy as np
from jax import lax
from jax.sharding import Mesh, PartitionSpec as P

DN = 128
DR = 64
DV = 128
QB = 96


NEG_FILL = -1e30
BLK = ("bz", "by")
HEAD = ("hh", "hc")


def swap_cores(value):
    return lax.ppermute(value, "hc", [(0, 1), (1, 0)])


def gather_blk(flat):
    nz, ny = lax.axis_size("bz"), lax.axis_size("by")
    step = lax.all_to_all(jnp.broadcast_to(flat[None], (nz,) + flat.shape), "bz", 0, 0, tiled=False)
    step = lax.all_to_all(jnp.broadcast_to(step[None], (ny,) + step.shape), "by", 0, 0, tiled=False)
    return jnp.transpose(step, (1, 0, 2)).reshape(nz * ny, flat.shape[0])


def per_device(query_heads, latent_cache, rope_keys, up_weight, out_weight, block_mask):
    tok_rows = query_heads.shape[0]
    head_count = out_weight.shape[0] // DV
    blk_count = lax.axis_size("bz") * lax.axis_size("by")
    chips = lax.axis_size("hh")
    my_index = lax.axis_index("bz") * lax.axis_size("by") + lax.axis_index("by")
    core = lax.axis_index("hc")
    all_tokens = tok_rows * blk_count
    half = tok_rows // 2
    kvr = latent_cache.shape[1]
    queries = query_heads.reshape(tok_rows, head_count, DN + DR)
    score_scale = 1.0 / math.sqrt(DN + DR)

    payload = jnp.concatenate([latent_cache, rope_keys], axis=1)
    mine = lax.dynamic_slice_in_dim(payload, core * half, half, 0)
    sizes = (up_weight.size, mine.size)
    flat = jnp.concatenate([up_weight.reshape(-1), mine.reshape(-1)])
    gathered = gather_blk(flat)
    full_up = gathered[:, : sizes[0]].reshape(-1, up_weight.shape[1])
    mine_all = gathered[:, sizes[0]:].reshape(blk_count * half, payload.shape[1])
    theirs_all = swap_cores(mine_all)
    payload_all = jnp.concatenate([mine_all, theirs_all], axis=0)
    latent_all = payload_all[:, :kvr]
    rope_all = payload_all[:, kvr:]

    row = jnp.arange(blk_count * half, dtype=jnp.int32)
    block_start = (row // half) * tok_rows + row % half
    key_pos = jnp.concatenate([block_start + core * half, block_start + (1 - core) * half])
    query_pos = my_index * tok_rows + jnp.arange(tok_rows, dtype=jnp.int32)
    mask_rows = lax.dynamic_slice_in_dim(block_mask, my_index * (tok_rows // QB), tok_rows // QB, 0)
    bits = jnp.take(mask_rows, key_pos // QB, axis=1)
    bits = jnp.repeat(bits, QB, axis=0) == 1
    allowed = bits & (key_pos[None, :] <= query_pos[:, None])

    def attend(operands):
        query_part, up_part = operands
        per = query_part.shape[1]
        expanded = jnp.dot(latent_all, up_part, preferred_element_type=jnp.float32).astype(jnp.bfloat16)
        expanded = expanded.reshape(all_tokens, per, DN + DV)
        scores = jnp.einsum(
            "qhd,khd->hqk", query_part[:, :, :DN], expanded[:, :, :DN], preferred_element_type=jnp.float32
        )
        scores = scores + jnp.einsum(
            "qhr,kr->hqk", query_part[:, :, DN:], rope_all, preferred_element_type=jnp.float32
        )
        scores = jnp.where(allowed[None], scores * score_scale, NEG_FILL)
        row_max = jnp.max(scores, axis=2, keepdims=True)
        weights = jnp.where(allowed[None], jnp.exp(scores - row_max), 0.0)
        denominator = jnp.sum(weights, axis=2)
        mixed = jnp.einsum(
            "hqk,khv->hqv",
            weights.astype(jnp.bfloat16),
            expanded[:, :, DN:],
            preferred_element_type=jnp.float32,
        )
        return (mixed / denominator[:, :, None]).astype(jnp.bfloat16)

    chunks = 2
    per = head_count // chunks
    query_chunks = jnp.transpose(queries.reshape(tok_rows, chunks, per, DN + DR), (1, 0, 2, 3))
    up_chunks = jnp.transpose(full_up.reshape(kvr, chunks, per * (DN + DV)), (1, 0, 2))
    outputs = lax.map(attend, (query_chunks, up_chunks))
    outputs = jnp.transpose(outputs.reshape(head_count, tok_rows, DV), (1, 0, 2))
    outputs = outputs.reshape(tok_rows, head_count * DV)

    split_w = out_weight.reshape(out_weight.shape[0], chips, 2, -1)
    part = [
        jnp.einsum("qr,rhc->qhc", outputs, split_w[:, :, c, :], preferred_element_type=jnp.float32)
        .astype(jnp.bfloat16)
        for c in range(2)
    ]
    keep = jnp.where(core == 0, part[0], part[1])
    give = jnp.where(core == 0, part[1], part[0])
    paired = (keep.astype(jnp.float32) + swap_cores(give).astype(jnp.float32)).astype(jnp.bfloat16)
    paired = lax.all_to_all(paired, "hh", 1, 1, tiled=False)
    return paired.astype(jnp.float32).sum(axis=1).astype(jnp.bfloat16)


def solution(mesh):
    blk, heads = mesh.devices.shape
    split = Mesh(np.asarray(mesh.devices).reshape(4, blk // 4, heads // 2, 2), BLK + HEAD)
    return jax.shard_map(
        per_device,
        mesh=split,
        in_specs=(
            P(BLK, HEAD),
            P(BLK, None),
            P(BLK, None),
            P(BLK, HEAD),
            P(HEAD, None),
            P(),
        ),
        out_specs=P(BLK, HEAD),
        check_vma=False,
    )
```

```python
import math

import jax
import jax.numpy as jnp
import numpy as np
from jax import lax
from jax.sharding import Mesh, PartitionSpec as P

DN = 128
DR = 64
DV = 128
QB = 96


NEG_FILL = -1e30
HEAD = ("hh", "hc")


def per_device(query_heads, latent_cache, rope_keys, up_weight, out_weight, block_mask):
    tok_rows = query_heads.shape[0]
    head_count = out_weight.shape[0] // DV
    blk_count = lax.axis_size("blk")
    chips = lax.axis_size("hh")
    my_index = lax.axis_index("blk")
    core = lax.axis_index("hc")
    all_tokens = tok_rows * blk_count
    half = tok_rows // 2
    kvr = latent_cache.shape[1]
    queries = query_heads.reshape(tok_rows, head_count, DN + DR)
    query_nope = queries[:, :, :DN]
    query_rot = queries[:, :, DN:]
    score_scale = 1.0 / math.sqrt(DN + DR)

    full_up = lax.all_gather(up_weight, "blk", axis=0, tiled=True)

    payload = jnp.concatenate([latent_cache, rope_keys], axis=1)
    mine = lax.dynamic_slice_in_dim(payload, core * half, half, 0)
    spread = jnp.broadcast_to(mine[None], (blk_count,) + mine.shape)
    mine_all = lax.all_to_all(spread, "blk", 0, 0, tiled=False).reshape(blk_count * half, -1)
    theirs_all = lax.ppermute(mine_all, "hc", [(0, 1), (1, 0)])
    payload_all = jnp.concatenate([mine_all, theirs_all], axis=0)
    latent_all = payload_all[:, :kvr]
    rope_all = payload_all[:, kvr:]

    expanded = jnp.dot(latent_all, full_up, preferred_element_type=jnp.float32).astype(jnp.bfloat16)
    expanded = expanded.reshape(all_tokens, head_count, DN + DV)

    row = jnp.arange(blk_count * half, dtype=jnp.int32)
    block_start = (row // half) * tok_rows + row % half
    key_pos = jnp.concatenate([block_start + core * half, block_start + (1 - core) * half])
    query_pos = my_index * tok_rows + jnp.arange(tok_rows, dtype=jnp.int32)
    mask_rows = lax.dynamic_slice_in_dim(block_mask, my_index * (tok_rows // QB), tok_rows // QB, 0)
    bits = jnp.take(mask_rows, key_pos // QB, axis=1)
    bits = jnp.repeat(bits, QB, axis=0) == 1
    allowed = bits & (key_pos[None, :] <= query_pos[:, None])

    scores = jnp.einsum(
        "qhd,khd->hqk", query_nope, expanded[:, :, :DN], preferred_element_type=jnp.float32
    )
    scores = scores + jnp.einsum(
        "qhr,kr->hqk", query_rot, rope_all, preferred_element_type=jnp.float32
    )
    scores = jnp.where(allowed[None], scores * score_scale, NEG_FILL)
    row_max = jnp.max(scores, axis=2, keepdims=True)
    weights = jnp.where(allowed[None], jnp.exp(scores - row_max), 0.0)
    denominator = jnp.sum(weights, axis=2)
    mixed = jnp.einsum(
        "hqk,khv->hqv",
        weights.astype(jnp.bfloat16),
        expanded[:, :, DN:],
        preferred_element_type=jnp.float32,
    )
    outputs = (mixed / denominator[:, :, None]).astype(jnp.bfloat16)
    outputs = jnp.transpose(outputs, (1, 0, 2)).reshape(tok_rows, head_count * DV)
    partial_sum = jnp.dot(outputs, out_weight, preferred_element_type=jnp.float32).astype(jnp.bfloat16)

    pieces = partial_sum.reshape(tok_rows, chips, 2, -1)
    pieces = lax.all_to_all(pieces, "hc", 2, 2, tiled=False)
    paired = pieces.astype(jnp.float32).sum(axis=2).astype(jnp.bfloat16)
    paired = lax.all_to_all(paired, "hh", 1, 1, tiled=False)
    return paired.astype(jnp.float32).sum(axis=1).astype(jnp.bfloat16)


def solution(mesh):
    blk, heads = mesh.devices.shape
    split = Mesh(np.asarray(mesh.devices).reshape(blk, heads // 2, 2), ("blk",) + HEAD)
    return jax.shard_map(
        per_device,
        mesh=split,
        in_specs=(
            P("blk", HEAD),
            P("blk", None),
            P("blk", None),
            P("blk", HEAD),
            P(HEAD, None),
            P(),
        ),
        out_specs=P("blk", HEAD),
        check_vma=False,
    )
```

```python
import math

import jax
import jax.numpy as jnp
import numpy as np
from jax import lax
from jax.experimental import pallas as pl
from jax.experimental.pallas import tpu as pltpu
from jax.sharding import Mesh, PartitionSpec as P

DN = 128
DR = 64
DV = 128
QB = 96


NEG_FILL = -1e30
HEAD = ("hh", "hc")


def attn_kernel(scale, qn_ref, qr_ref, k_ref, v_ref, rope_ref, mask_ref, o_ref):
    nt = (((1,), (1,)), ((), ()))
    s = lax.dot_general(qn_ref[0], k_ref[...], nt, preferred_element_type=jnp.float32)
    s = s + lax.dot_general(qr_ref[0], rope_ref[...], nt, preferred_element_type=jnp.float32)
    allowed = mask_ref[...] != 0
    s = jnp.where(allowed, s * scale, NEG_FILL)
    m = jnp.max(s, axis=1, keepdims=True)
    p = jnp.where(allowed, jnp.exp(s - m), 0.0)
    l = jnp.sum(p, axis=1, keepdims=True)
    o = jnp.dot(p.astype(jnp.bfloat16), v_ref[...], preferred_element_type=jnp.float32)
    o_ref[...] = (o / l).astype(o_ref.dtype)

def attention(q_nope, q_rot, expanded, rope_all, mask):
    heads, tok, _ = q_nope.shape
    keys = expanded.shape[0]
    scale = 1.0 / math.sqrt(DN + DR)
    return pl.pallas_call(
        lambda *r: attn_kernel(scale, *r),
        grid=(heads,),
        in_specs=[
            pl.BlockSpec((1, tok, DN), lambda h: (h, 0, 0)),
            pl.BlockSpec((1, tok, DR), lambda h: (h, 0, 0)),
            pl.BlockSpec((keys, DN), lambda h: (0, 2 * h)),
            pl.BlockSpec((keys, DV), lambda h: (0, 2 * h + 1)),
            pl.BlockSpec((keys, DR), lambda h: (0, 0)),
            pl.BlockSpec((tok, keys), lambda h: (0, 0)),
        ],
        out_specs=pl.BlockSpec((tok, DV), lambda h: (0, h)),
        out_shape=jax.ShapeDtypeStruct((tok, heads * DV), jnp.bfloat16),
        compiler_params=pltpu.CompilerParams(dimension_semantics=("arbitrary",)),
        cost_estimate=pl.CostEstimate(
            flops=2 * heads * tok * keys * (DN + DR + DV),
            transcendentals=heads * tok * keys,
            bytes_accessed=2 * (expanded.size + heads * tok * (DN + DR + DV) + rope_all.size) + 4 * mask.size,
        ),
    )(q_nope, q_rot, expanded, expanded, rope_all, mask)


def per_device(query_heads, latent_cache, rope_keys, up_weight, out_weight, block_mask):
    tok_rows = query_heads.shape[0]
    head_count = out_weight.shape[0] // DV
    blk_count = lax.axis_size("blk")
    chips = lax.axis_size("hh")
    my_index = lax.axis_index("blk")
    core = lax.axis_index("hc")
    all_tokens = tok_rows * blk_count
    half = tok_rows // 2
    kvr = latent_cache.shape[1]
    queries = query_heads.reshape(tok_rows, head_count, DN + DR)

    full_up = lax.all_gather(up_weight, "blk", axis=0, tiled=True)

    payload = jnp.concatenate([latent_cache, rope_keys], axis=1)
    mine = lax.dynamic_slice_in_dim(payload, core * half, half, 0)
    spread = jnp.broadcast_to(mine[None], (blk_count,) + mine.shape)
    mine_all = lax.all_to_all(spread, "blk", 0, 0, tiled=False).reshape(blk_count * half, -1)
    theirs_all = lax.ppermute(mine_all, "hc", [(0, 1), (1, 0)])
    payload_all = jnp.concatenate([mine_all, theirs_all], axis=0)
    latent_all = payload_all[:, :kvr]
    rope_all = payload_all[:, kvr:]

    expanded = jnp.dot(latent_all, full_up, preferred_element_type=jnp.float32).astype(jnp.bfloat16)

    row = jnp.arange(blk_count * half, dtype=jnp.int32)
    block_start = (row // half) * tok_rows + row % half
    key_pos = jnp.concatenate([block_start + core * half, block_start + (1 - core) * half])
    query_pos = my_index * tok_rows + jnp.arange(tok_rows, dtype=jnp.int32)
    q_blocks = tok_rows // QB
    mask_rows = lax.dynamic_slice_in_dim(block_mask, my_index * q_blocks, q_blocks, 0)
    by_half = mask_rows.reshape(q_blocks, blk_count, 2)
    mine_bits = jnp.where(core == 0, by_half[:, :, 0], by_half[:, :, 1])
    theirs_bits = jnp.where(core == 0, by_half[:, :, 1], by_half[:, :, 0])
    bits = jnp.stack([mine_bits, theirs_bits], axis=1)
    bits = jnp.broadcast_to(bits[:, None, :, :, None], (q_blocks, QB, 2, blk_count, half // QB * QB))
    bits = bits.reshape(tok_rows, all_tokens) == 1
    allowed = (bits & (key_pos[None, :] <= query_pos[:, None])).astype(jnp.int32)

    q_nope = jnp.transpose(queries[:, :, :DN], (1, 0, 2))
    q_rot = jnp.transpose(queries[:, :, DN:], (1, 0, 2))
    outputs = attention(q_nope, q_rot, expanded, rope_all, allowed)
    partial_sum = jnp.dot(outputs, out_weight, preferred_element_type=jnp.float32).astype(jnp.bfloat16)

    pieces = partial_sum.reshape(tok_rows, chips, 2, -1)
    pieces = lax.all_to_all(pieces, "hc", 2, 2, tiled=False)
    paired = pieces.astype(jnp.float32).sum(axis=2).astype(jnp.bfloat16)
    paired = lax.all_to_all(paired, "hh", 1, 1, tiled=False)
    return paired.astype(jnp.float32).sum(axis=1).astype(jnp.bfloat16)


def solution(mesh):
    blk, heads = mesh.devices.shape
    split = Mesh(np.asarray(mesh.devices).reshape(blk, heads // 2, 2), ("blk",) + HEAD)
    return jax.shard_map(
        per_device,
        mesh=split,
        in_specs=(
            P("blk", HEAD),
            P("blk", None),
            P("blk", None),
            P("blk", HEAD),
            P(HEAD, None),
            P(),
        ),
        out_specs=P("blk", HEAD),
        check_vma=False,
    )
```

```python
import math

import jax
import jax.numpy as jnp
import numpy as np
from jax import lax
from jax.experimental import pallas as pl
from jax.experimental.pallas import tpu as pltpu
from jax.sharding import Mesh, PartitionSpec as P


DN = 128
DR = 64
DV = 128
QB = 96


NEG_FILL = -1e30
HEAD = ("hh", "hc")


def attn_kernel(scale, qn_ref, qr_ref, k_ref, v_ref, rope_ref, mask_ref, o_ref):
    nt = (((1,), (1,)), ((), ()))
    s = lax.dot_general(qn_ref[0], k_ref[...], nt, preferred_element_type=jnp.float32)
    s = s + lax.dot_general(qr_ref[0], rope_ref[...], nt, preferred_element_type=jnp.float32)
    allowed = mask_ref[...] != 0
    s = jnp.where(allowed, s * scale, NEG_FILL)
    m = jnp.max(s, axis=1, keepdims=True)
    p = jnp.where(allowed, jnp.exp(s - m), 0.0)
    l = jnp.sum(p, axis=1, keepdims=True)
    o = jnp.dot(p.astype(jnp.bfloat16), v_ref[...], preferred_element_type=jnp.float32)
    o_ref[...] = (o / l).astype(o_ref.dtype)


def attention(q_nope, q_rot, expanded, rope_all, mask):
    heads, tok, _ = q_nope.shape
    keys = expanded.shape[0]
    scale = 1.0 / math.sqrt(DN + DR)
    return pl.pallas_call(
        lambda *r: attn_kernel(scale, *r),
        grid=(heads,),
        in_specs=[
            pl.BlockSpec((1, tok, DN), lambda h: (h, 0, 0)),
            pl.BlockSpec((1, tok, DR), lambda h: (h, 0, 0)),
            pl.BlockSpec((keys, DN), lambda h: (0, 2 * h)),
            pl.BlockSpec((keys, DV), lambda h: (0, 2 * h + 1)),
            pl.BlockSpec((keys, DR), lambda h: (0, 0)),
            pl.BlockSpec((tok, keys), lambda h: (0, 0)),
        ],
        out_specs=pl.BlockSpec((tok, DV), lambda h: (0, h)),
        out_shape=jax.ShapeDtypeStruct((tok, heads * DV), jnp.bfloat16),
        compiler_params=pltpu.CompilerParams(dimension_semantics=("arbitrary",)),
        cost_estimate=pl.CostEstimate(
            flops=2 * heads * tok * keys * (DN + DR + DV),
            transcendentals=heads * tok * keys,
            bytes_accessed=2 * (expanded.size + heads * tok * (DN + DR + DV) + rope_all.size) + 4 * mask.size,
        ),
    )(q_nope, q_rot, expanded, expanded, rope_all, mask)


def per_device(query_heads, latent_cache, rope_keys, up_weight, out_weight, block_mask):
    tok_rows = query_heads.shape[0]
    head_count = out_weight.shape[0] // DV
    blk_count = lax.axis_size("blk")
    chips = lax.axis_size("hh")
    my_index = lax.axis_index("blk")
    core = lax.axis_index("hc")
    all_tokens = tok_rows * blk_count
    half = tok_rows // 2
    kvr = latent_cache.shape[1]
    queries = query_heads.reshape(tok_rows, head_count, DN + DR)

    full_up = lax.all_gather(up_weight, "blk", axis=0, tiled=True)

    payload = jnp.concatenate([latent_cache, rope_keys], axis=1)
    mine = lax.dynamic_slice_in_dim(payload, core * half, half, 0)
    spread = jnp.broadcast_to(mine[None], (blk_count,) + mine.shape)
    mine_all = lax.all_to_all(spread, "blk", 0, 0, tiled=False).reshape(blk_count * half, -1)
    theirs_all = lax.ppermute(mine_all, "hc", [(0, 1), (1, 0)])
    payload_all = jnp.concatenate([mine_all, theirs_all], axis=0)
    latent_all = payload_all[:, :kvr]
    rope_all = payload_all[:, kvr:]

    expanded = jnp.dot(latent_all, full_up, preferred_element_type=jnp.float32).astype(jnp.bfloat16)

    row = jnp.arange(blk_count * half, dtype=jnp.int32)
    block_start = (row // half) * tok_rows + row % half
    key_pos = jnp.concatenate([block_start + core * half, block_start + (1 - core) * half])
    query_pos = my_index * tok_rows + jnp.arange(tok_rows, dtype=jnp.int32)
    q_blocks = tok_rows // QB
    mask_rows = lax.dynamic_slice_in_dim(block_mask, my_index * q_blocks, q_blocks, 0)
    by_half = mask_rows.reshape(q_blocks, blk_count, 2)
    mine_bits = jnp.where(core == 0, by_half[:, :, 0], by_half[:, :, 1])
    theirs_bits = jnp.where(core == 0, by_half[:, :, 1], by_half[:, :, 0])
    bits = jnp.stack([mine_bits, theirs_bits], axis=1)
    bits = jnp.broadcast_to(bits[:, None, :, :, None], (q_blocks, QB, 2, blk_count, half // QB * QB))
    bits = bits.reshape(tok_rows, all_tokens) == 1
    allowed = (bits & (key_pos[None, :] <= query_pos[:, None])).astype(jnp.int32)

    q_nope = jnp.transpose(queries[:, :, :DN], (1, 0, 2))
    q_rot = jnp.transpose(queries[:, :, DN:], (1, 0, 2))
    outputs = attention(q_nope, q_rot, expanded, rope_all, allowed)
    partial_sum = jnp.dot(outputs, out_weight, preferred_element_type=jnp.float32).astype(jnp.bfloat16)

    split_w = out_weight.reshape(out_weight.shape[0], chips, 2, -1)
    pieces = jnp.einsum("qr,rhcd->chqd", outputs, split_w, preferred_element_type=jnp.float32)
    pieces = lax.all_to_all(pieces.astype(jnp.bfloat16), "hc", 0, 0, tiled=False)
    paired = pieces.astype(jnp.float32).sum(axis=0).astype(jnp.bfloat16)
    paired = lax.all_to_all(paired, "hh", 0, 0, tiled=False)
    return paired.astype(jnp.float32).sum(axis=0).astype(jnp.bfloat16)


def solution(mesh):
    blk, heads = mesh.devices.shape
    split = Mesh(np.asarray(mesh.devices).reshape(blk, heads // 2, 2), ("blk",) + HEAD)
    return jax.shard_map(
        per_device,
        mesh=split,
        in_specs=(
            P("blk", HEAD),
            P("blk", None),
            P("blk", None),
            P("blk", HEAD),
            P(HEAD, None),
            P(),
        ),
        out_specs=P("blk", HEAD),
        check_vma=False,
    )
```

```python
import math

import jax
import jax.numpy as jnp
import numpy as np
from jax import lax
from jax.experimental import pallas as pl
from jax.experimental.pallas import tpu as pltpu
from jax.sharding import Mesh, PartitionSpec as P

DN = 128
DR = 64
DV = 128
QB = 96


NEG_FILL = -1e30
HEAD = ("hh", "hc")


def attn_kernel(scale, qn_ref, qr_ref, lat_ref, up_ref, rope_ref, bias_ref, o_ref):
    nt = (((1,), (1,)), ((), ()))
    latent = lat_ref[...]
    keys = jnp.dot(latent, up_ref[:, :DN], preferred_element_type=jnp.float32).astype(jnp.bfloat16)
    s = lax.dot_general(qn_ref[0], keys, nt, preferred_element_type=jnp.float32)
    s = s + lax.dot_general(qr_ref[0], rope_ref[...], nt, preferred_element_type=jnp.float32)
    s = s * scale + bias_ref[...]
    m = jnp.max(s, axis=1, keepdims=True)
    p = jnp.exp(s - m)
    l = jnp.sum(p, axis=1, keepdims=True)
    values = jnp.dot(latent, up_ref[:, DN:], preferred_element_type=jnp.float32).astype(jnp.bfloat16)
    o = jnp.dot(p.astype(jnp.bfloat16), values, preferred_element_type=jnp.float32)
    o_ref[...] = (o / l).astype(o_ref.dtype)


def attention(q_nope, q_rot, latent_all, full_up, rope_all, bias):
    heads, tok, _ = q_nope.shape
    keys, kvr = latent_all.shape
    scale = 1.0 / math.sqrt(DN + DR)
    return pl.pallas_call(
        lambda *r: attn_kernel(scale, *r),
        grid=(heads,),
        in_specs=[
            pl.BlockSpec((1, tok, DN), lambda h: (h, 0, 0)),
            pl.BlockSpec((1, tok, DR), lambda h: (h, 0, 0)),
            pl.BlockSpec((keys, kvr), lambda h: (0, 0)),
            pl.BlockSpec((kvr, DN + DV), lambda h: (0, h)),
            pl.BlockSpec((keys, DR), lambda h: (0, 0)),
            pl.BlockSpec((tok, keys), lambda h: (0, 0)),
        ],
        out_specs=pl.BlockSpec((tok, DV), lambda h: (0, h)),
        out_shape=jax.ShapeDtypeStruct((tok, heads * DV), jnp.bfloat16),
        compiler_params=pltpu.CompilerParams(
            dimension_semantics=("arbitrary",), vmem_limit_bytes=48 * 1024 * 1024
        ),
        cost_estimate=pl.CostEstimate(
            flops=2 * heads * keys * (kvr * (DN + DV) + tok * (DN + DR + DV)),
            transcendentals=heads * tok * keys,
            bytes_accessed=2 * (latent_all.size + full_up.size + heads * tok * (DN + DR + DV) + rope_all.size)
            + 4 * bias.size,
        ),
    )(q_nope, q_rot, latent_all, full_up, rope_all, bias)


def per_device(query_heads, latent_cache, rope_keys, up_weight, out_weight, block_mask):
    tok_rows = query_heads.shape[0]
    head_count = out_weight.shape[0] // DV
    blk_count = lax.axis_size("blk")
    chips = lax.axis_size("hh")
    my_index = lax.axis_index("blk")
    core = lax.axis_index("hc")
    all_tokens = tok_rows * blk_count
    half = tok_rows // 2
    kvr = latent_cache.shape[1]
    queries = query_heads.reshape(tok_rows, head_count, DN + DR)

    full_up = lax.all_gather(up_weight, "blk", axis=0, tiled=True)

    payload = jnp.concatenate([latent_cache, rope_keys], axis=1)
    mine = lax.dynamic_slice_in_dim(payload, core * half, half, 0)
    spread = jnp.broadcast_to(mine[None], (blk_count,) + mine.shape)
    mine_all = lax.all_to_all(spread, "blk", 0, 0, tiled=False).reshape(blk_count * half, -1)
    theirs_all = lax.ppermute(mine_all, "hc", [(0, 1), (1, 0)])
    payload_all = jnp.concatenate([mine_all, theirs_all], axis=0)
    latent_all = payload_all[:, :kvr]
    rope_all = payload_all[:, kvr:]

    row = jnp.arange(blk_count * half, dtype=jnp.int32)
    block_start = (row // half) * tok_rows + row % half
    key_pos = jnp.concatenate([block_start + core * half, block_start + (1 - core) * half])
    query_pos = my_index * tok_rows + jnp.arange(tok_rows, dtype=jnp.int32)
    q_blocks = tok_rows // QB
    mask_rows = lax.dynamic_slice_in_dim(block_mask, my_index * q_blocks, q_blocks, 0)
    by_half = mask_rows.reshape(q_blocks, blk_count, 2)
    mine_bits = jnp.where(core == 0, by_half[:, :, 0], by_half[:, :, 1])
    theirs_bits = jnp.where(core == 0, by_half[:, :, 1], by_half[:, :, 0])
    bits = jnp.stack([mine_bits, theirs_bits], axis=1)
    bits = jnp.broadcast_to(bits[:, None, :, :, None], (q_blocks, QB, 2, blk_count, half // QB * QB))
    bits = bits.reshape(tok_rows, all_tokens) == 1
    allowed = bits & (key_pos[None, :] <= query_pos[:, None])
    bias = jnp.where(allowed, 0.0, NEG_FILL).astype(jnp.float32)

    q_nope = jnp.transpose(queries[:, :, :DN], (1, 0, 2))
    q_rot = jnp.transpose(queries[:, :, DN:], (1, 0, 2))
    outputs = attention(q_nope, q_rot, latent_all, full_up, rope_all, bias)
    partial_sum = jnp.dot(outputs, out_weight, preferred_element_type=jnp.float32).astype(jnp.bfloat16)

    pieces = partial_sum.reshape(tok_rows, chips, 2, -1)
    pieces = lax.all_to_all(pieces, "hc", 2, 2, tiled=False)
    paired = pieces.astype(jnp.float32).sum(axis=2).astype(jnp.bfloat16)
    paired = lax.all_to_all(paired, "hh", 1, 1, tiled=False)
    return paired.astype(jnp.float32).sum(axis=1).astype(jnp.bfloat16)


def solution(mesh):
    blk, heads = mesh.devices.shape
    split = Mesh(np.asarray(mesh.devices).reshape(blk, heads // 2, 2), ("blk",) + HEAD)
    return jax.shard_map(
        per_device,
        mesh=split,
        in_specs=(
            P("blk", HEAD),
            P("blk", None),
            P("blk", None),
            P("blk", HEAD),
            P(HEAD, None),
            P(),
        ),
        out_specs=P("blk", HEAD),
        check_vma=False,
    )
```

```python
import math

import jax
import jax.numpy as jnp
import numpy as np
from jax import lax
from jax.experimental import pallas as pl
from jax.experimental.pallas import tpu as pltpu
from jax.sharding import Mesh, PartitionSpec as P

DN = 128
DR = 64
DV = 128
QB = 96


NEG_FILL = -1e30
HEAD = ("hh", "hc")


def attn_kernel(scale, qn_ref, qr_ref, k_ref, v_ref, rope_ref, bias_ref, o_ref):
    nt = (((1,), (1,)), ((), ()))
    s = lax.dot_general(qn_ref[0], k_ref[...], nt, preferred_element_type=jnp.float32)
    s = s + lax.dot_general(qr_ref[0], rope_ref[...], nt, preferred_element_type=jnp.float32)
    s = s * scale + bias_ref[...]
    m = jnp.max(s, axis=1, keepdims=True)
    p = jnp.exp(s - m)
    l = jnp.sum(p, axis=1, keepdims=True)
    o = jnp.dot(p.astype(jnp.bfloat16), v_ref[...], preferred_element_type=jnp.float32)
    o_ref[...] = (o / l).astype(o_ref.dtype)

def attention(q_nope, q_rot, expanded, rope_all, mask):
    heads, tok, _ = q_nope.shape
    keys = expanded.shape[0]
    scale = 1.0 / math.sqrt(DN + DR)
    return pl.pallas_call(
        lambda *r: attn_kernel(scale, *r),
        grid=(heads,),
        in_specs=[
            pl.BlockSpec((1, tok, DN), lambda h: (h, 0, 0)),
            pl.BlockSpec((1, tok, DR), lambda h: (h, 0, 0)),
            pl.BlockSpec((keys, DN), lambda h: (0, 2 * h)),
            pl.BlockSpec((keys, DV), lambda h: (0, 2 * h + 1)),
            pl.BlockSpec((keys, DR), lambda h: (0, 0)),
            pl.BlockSpec((tok, keys), lambda h: (0, 0)),
        ],
        out_specs=pl.BlockSpec((tok, DV), lambda h: (0, h)),
        out_shape=jax.ShapeDtypeStruct((tok, heads * DV), jnp.bfloat16),
        compiler_params=pltpu.CompilerParams(dimension_semantics=("arbitrary",)),
        cost_estimate=pl.CostEstimate(
            flops=2 * heads * tok * keys * (DN + DR + DV),
            transcendentals=heads * tok * keys,
            bytes_accessed=2 * (expanded.size + heads * tok * (DN + DR + DV) + rope_all.size) + 4 * mask.size,
        ),
    )(q_nope, q_rot, expanded, expanded, rope_all, mask)


def per_device(query_heads, latent_cache, rope_keys, up_weight, out_weight, block_mask):
    tok_rows = query_heads.shape[0]
    head_count = out_weight.shape[0] // DV
    blk_count = lax.axis_size("blk")
    chips = lax.axis_size("hh")
    my_index = lax.axis_index("blk")
    core = lax.axis_index("hc")
    all_tokens = tok_rows * blk_count
    half = tok_rows // 2
    kvr = latent_cache.shape[1]
    queries = query_heads.reshape(tok_rows, head_count, DN + DR)

    full_up = lax.all_gather(up_weight, "blk", axis=0, tiled=True)

    payload = jnp.concatenate([latent_cache, rope_keys], axis=1)
    mine = lax.dynamic_slice_in_dim(payload, core * half, half, 0)
    spread = jnp.broadcast_to(mine[None], (blk_count,) + mine.shape)
    mine_all = lax.all_to_all(spread, "blk", 0, 0, tiled=False).reshape(blk_count * half, -1)
    theirs_all = lax.ppermute(mine_all, "hc", [(0, 1), (1, 0)])
    payload_all = jnp.concatenate([mine_all, theirs_all], axis=0)
    latent_all = payload_all[:, :kvr]
    rope_all = payload_all[:, kvr:]

    expanded = jnp.dot(latent_all, full_up, preferred_element_type=jnp.float32).astype(jnp.bfloat16)

    row = jnp.arange(blk_count * half, dtype=jnp.int32)
    block_start = (row // half) * tok_rows + row % half
    key_pos = jnp.concatenate([block_start + core * half, block_start + (1 - core) * half])
    query_pos = my_index * tok_rows + jnp.arange(tok_rows, dtype=jnp.int32)
    q_blocks = tok_rows // QB
    mask_rows = lax.dynamic_slice_in_dim(block_mask, my_index * q_blocks, q_blocks, 0)
    by_half = mask_rows.reshape(q_blocks, blk_count, 2)
    mine_bits = jnp.where(core == 0, by_half[:, :, 0], by_half[:, :, 1])
    theirs_bits = jnp.where(core == 0, by_half[:, :, 1], by_half[:, :, 0])
    bits = jnp.stack([mine_bits, theirs_bits], axis=1)
    bits = jnp.broadcast_to(bits[:, None, :, :, None], (q_blocks, QB, 2, blk_count, half // QB * QB))
    bits = bits.reshape(tok_rows, all_tokens) == 1
    allowed = bits & (key_pos[None, :] <= query_pos[:, None])
    bias = jnp.where(allowed, 0.0, NEG_FILL).astype(jnp.float32)

    q_nope = jnp.transpose(queries[:, :, :DN], (1, 0, 2))
    q_rot = jnp.transpose(queries[:, :, DN:], (1, 0, 2))
    outputs = attention(q_nope, q_rot, expanded, rope_all, bias)
    partial_sum = jnp.dot(outputs, out_weight, preferred_element_type=jnp.float32).astype(jnp.bfloat16)

    pieces = partial_sum.reshape(tok_rows, chips, 2, -1)
    pieces = lax.all_to_all(pieces, "hc", 2, 2, tiled=False)
    paired = pieces.astype(jnp.float32).sum(axis=2).astype(jnp.bfloat16)
    paired = lax.all_to_all(paired, "hh", 1, 1, tiled=False)
    return paired.astype(jnp.float32).sum(axis=1).astype(jnp.bfloat16)


def solution(mesh):
    blk, heads = mesh.devices.shape
    split = Mesh(np.asarray(mesh.devices).reshape(blk, heads // 2, 2), ("blk",) + HEAD)
    return jax.shard_map(
        per_device,
        mesh=split,
        in_specs=(
            P("blk", HEAD),
            P("blk", None),
            P("blk", None),
            P("blk", HEAD),
            P(HEAD, None),
            P(),
        ),
        out_specs=P("blk", HEAD),
        check_vma=False,
    )
```

```python
import math

import jax
import jax.numpy as jnp
import numpy as np
from jax import lax
from jax.experimental import pallas as pl
from jax.experimental.pallas import tpu as pltpu
from jax.sharding import Mesh, PartitionSpec as P


DN = 128
DR = 64
DV = 128
QB = 96


NEG_FILL = -1e30
HEAD = ("hh", "hc")


def attn_kernel(scale, qn_ref, qr_ref, k_ref, v_ref, rope_ref, bias_ref, o_ref):
    nt = (((1,), (1,)), ((), ()))
    s = lax.dot_general(qn_ref[0], k_ref[...], nt, preferred_element_type=jnp.float32)
    s = s + lax.dot_general(qr_ref[0], rope_ref[...], nt, preferred_element_type=jnp.float32)
    s = s * scale + bias_ref[...]
    m = jnp.max(s, axis=1, keepdims=True)
    p = jnp.exp(s - m)
    l = jnp.sum(p, axis=1, keepdims=True)
    o = jnp.dot(p.astype(jnp.bfloat16), v_ref[...], preferred_element_type=jnp.float32)
    o_ref[...] = (o / l).astype(o_ref.dtype)


def attention(q_nope, q_rot, expanded, rope_all, mask):
    heads, tok, _ = q_nope.shape
    keys = expanded.shape[0]
    scale = 1.0 / math.sqrt(DN + DR)
    return pl.pallas_call(
        lambda *r: attn_kernel(scale, *r),
        grid=(heads,),
        in_specs=[
            pl.BlockSpec((1, tok, DN), lambda h: (h, 0, 0)),
            pl.BlockSpec((1, tok, DR), lambda h: (h, 0, 0)),
            pl.BlockSpec((keys, DN), lambda h: (0, 2 * h)),
            pl.BlockSpec((keys, DV), lambda h: (0, 2 * h + 1)),
            pl.BlockSpec((keys, DR), lambda h: (0, 0)),
            pl.BlockSpec((tok, keys), lambda h: (0, 0)),
        ],
        out_specs=pl.BlockSpec((tok, DV), lambda h: (0, h)),
        out_shape=jax.ShapeDtypeStruct((tok, heads * DV), jnp.bfloat16),
        compiler_params=pltpu.CompilerParams(dimension_semantics=("arbitrary",)),
        cost_estimate=pl.CostEstimate(
            flops=2 * heads * tok * keys * (DN + DR + DV),
            transcendentals=heads * tok * keys,
            bytes_accessed=2 * (expanded.size + heads * tok * (DN + DR + DV) + rope_all.size) + 4 * mask.size,
        ),
    )(q_nope, q_rot, expanded, expanded, rope_all, mask)


def per_device(query_heads, latent_cache, rope_keys, up_weight, out_weight, block_mask):
    tok_rows = query_heads.shape[0]
    head_count = out_weight.shape[0] // DV
    blk_count = lax.axis_size("blk")
    chips = lax.axis_size("hh")
    my_index = lax.axis_index("blk")
    core = lax.axis_index("hc")
    all_tokens = tok_rows * blk_count
    half = tok_rows // 2
    kvr = latent_cache.shape[1]
    queries = query_heads.reshape(tok_rows, head_count, DN + DR)

    full_up = lax.all_gather(up_weight, "blk", axis=0, tiled=True)

    payload = jnp.concatenate([latent_cache, rope_keys], axis=1)
    mine = lax.dynamic_slice_in_dim(payload, core * half, half, 0)
    spread = jnp.broadcast_to(mine[None], (blk_count,) + mine.shape)
    mine_all = lax.all_to_all(spread, "blk", 0, 0, tiled=False).reshape(blk_count * half, -1)
    theirs_all = lax.ppermute(mine_all, "hc", [(0, 1), (1, 0)])
    payload_all = jnp.concatenate([mine_all, theirs_all], axis=0)
    latent_all = payload_all[:, :kvr]
    rope_all = payload_all[:, kvr:]

    expanded = jnp.dot(latent_all, full_up, preferred_element_type=jnp.float32).astype(jnp.bfloat16)

    row = jnp.arange(blk_count * half, dtype=jnp.int32)
    block_start = (row // half) * tok_rows + row % half
    key_pos = jnp.concatenate([block_start + core * half, block_start + (1 - core) * half])
    query_pos = my_index * tok_rows + jnp.arange(tok_rows, dtype=jnp.int32)
    q_blocks = tok_rows // QB
    mask_rows = lax.dynamic_slice_in_dim(block_mask, my_index * q_blocks, q_blocks, 0)
    by_half = mask_rows.reshape(q_blocks, blk_count, 2)
    mine_bits = jnp.where(core == 0, by_half[:, :, 0], by_half[:, :, 1])
    theirs_bits = jnp.where(core == 0, by_half[:, :, 1], by_half[:, :, 0])
    bits = jnp.stack([mine_bits, theirs_bits], axis=1)
    bits = jnp.broadcast_to(bits[:, None, :, :, None], (q_blocks, QB, 2, blk_count, half // QB * QB))
    bits = bits.reshape(tok_rows, all_tokens) == 1
    allowed = bits & (key_pos[None, :] <= query_pos[:, None])
    bias = jnp.where(allowed, 0.0, NEG_FILL).astype(jnp.float32)

    q_nope = jnp.transpose(queries[:, :, :DN], (1, 0, 2))
    q_rot = jnp.transpose(queries[:, :, DN:], (1, 0, 2))

    def finish(rows):
        part = slice(rows * QB, (rows + 1) * QB)
        outputs = attention(q_nope[:, part], q_rot[:, part], expanded, rope_all, bias[part])
        partial_sum = jnp.dot(outputs, out_weight, preferred_element_type=jnp.float32).astype(jnp.bfloat16)
        pieces = partial_sum.reshape(QB, chips, 2, -1)
        pieces = lax.all_to_all(pieces, "hc", 2, 2, tiled=False)
        paired = pieces.astype(jnp.float32).sum(axis=2).astype(jnp.bfloat16)
        paired = lax.all_to_all(paired, "hh", 1, 1, tiled=False)
        return paired.astype(jnp.float32).sum(axis=1).astype(jnp.bfloat16)

    return jnp.concatenate([finish(rows) for rows in range(tok_rows // QB)], axis=0)


def solution(mesh):
    blk, heads = mesh.devices.shape
    split = Mesh(np.asarray(mesh.devices).reshape(blk, heads // 2, 2), ("blk",) + HEAD)
    return jax.shard_map(
        per_device,
        mesh=split,
        in_specs=(
            P("blk", HEAD),
            P("blk", None),
            P("blk", None),
            P("blk", HEAD),
            P(HEAD, None),
            P(),
        ),
        out_specs=P("blk", HEAD),
        check_vma=False,
    )
```

```python
import math

import jax
import jax.numpy as jnp
import numpy as np
from jax import lax
from jax.experimental import pallas as pl
from jax.experimental.pallas import tpu as pltpu
from jax.sharding import Mesh, PartitionSpec as P

DN = 128
DR = 64
DV = 128
QB = 96


NEG_FILL = -1e30
HEAD = ("hh", "hc")


def attn_kernel(scale, qn_ref, qr_ref, k_ref, v_ref, rope_ref, bias_ref, o_ref):
    nt = (((1,), (1,)), ((), ()))
    s = lax.dot_general(qn_ref[0], k_ref[...], nt, preferred_element_type=jnp.float32)
    s = s + lax.dot_general(qr_ref[0], rope_ref[...], nt, preferred_element_type=jnp.float32)
    s = s * scale + bias_ref[...]
    m = jnp.max(s, axis=1, keepdims=True)
    p = jnp.exp(s - m)
    l = jnp.sum(p, axis=1, keepdims=True)
    o = jnp.dot(p.astype(jnp.bfloat16), v_ref[...], preferred_element_type=jnp.float32)
    o_ref[...] = (o / l).astype(o_ref.dtype)

def attention(q_nope, q_rot, expanded, rope_all, mask):
    heads, tok, _ = q_nope.shape
    keys = expanded.shape[0]
    scale = 1.0 / math.sqrt(DN + DR)
    return pl.pallas_call(
        lambda *r: attn_kernel(scale, *r),
        grid=(heads,),
        in_specs=[
            pl.BlockSpec((1, tok, DN), lambda h: (h, 0, 0)),
            pl.BlockSpec((1, tok, DR), lambda h: (h, 0, 0)),
            pl.BlockSpec((keys, DN), lambda h: (0, 2 * h)),
            pl.BlockSpec((keys, DV), lambda h: (0, 2 * h + 1)),
            pl.BlockSpec((keys, DR), lambda h: (0, 0)),
            pl.BlockSpec((tok, keys), lambda h: (0, 0)),
        ],
        out_specs=pl.BlockSpec((tok, DV), lambda h: (0, h)),
        out_shape=jax.ShapeDtypeStruct((tok, heads * DV), jnp.bfloat16),
        compiler_params=pltpu.CompilerParams(dimension_semantics=("arbitrary",)),
        cost_estimate=pl.CostEstimate(
            flops=2 * heads * tok * keys * (DN + DR + DV),
            transcendentals=heads * tok * keys,
            bytes_accessed=2 * (expanded.size + heads * tok * (DN + DR + DV) + rope_all.size) + 4 * mask.size,
        ),
    )(q_nope, q_rot, expanded, expanded, rope_all, mask)


def per_device(query_heads, latent_cache, rope_keys, up_weight, out_weight, block_mask):
    tok_rows = query_heads.shape[0]
    head_count = out_weight.shape[0] // DV
    blk_count = lax.axis_size("blk")
    chips = lax.axis_size("hh")
    my_index = lax.axis_index("blk")
    core = lax.axis_index("hc")
    all_tokens = tok_rows * blk_count
    half = tok_rows // 2
    kvr = latent_cache.shape[1]
    queries = query_heads.reshape(tok_rows, head_count, DN + DR)

    payload = jnp.concatenate([latent_cache, rope_keys], axis=1)
    mine = lax.dynamic_slice_in_dim(payload, core * half, half, 0)
    flat = jnp.concatenate([up_weight.reshape(-1), mine.reshape(-1)])
    spread = jnp.broadcast_to(flat[None], (blk_count,) + flat.shape)
    gathered = lax.all_to_all(spread, "blk", 0, 0, tiled=False)
    full_up = gathered[:, : up_weight.size].reshape(-1, up_weight.shape[1])
    mine_all = gathered[:, up_weight.size:].reshape(blk_count * half, -1)
    theirs_all = lax.ppermute(mine_all, "hc", [(0, 1), (1, 0)])
    payload_all = jnp.concatenate([mine_all, theirs_all], axis=0)
    latent_all = payload_all[:, :kvr]
    rope_all = payload_all[:, kvr:]

    expanded = jnp.dot(latent_all, full_up, preferred_element_type=jnp.float32).astype(jnp.bfloat16)

    row = jnp.arange(blk_count * half, dtype=jnp.int32)
    block_start = (row // half) * tok_rows + row % half
    key_pos = jnp.concatenate([block_start + core * half, block_start + (1 - core) * half])
    query_pos = my_index * tok_rows + jnp.arange(tok_rows, dtype=jnp.int32)
    q_blocks = tok_rows // QB
    mask_rows = lax.dynamic_slice_in_dim(block_mask, my_index * q_blocks, q_blocks, 0)
    by_half = mask_rows.reshape(q_blocks, blk_count, 2)
    mine_bits = jnp.where(core == 0, by_half[:, :, 0], by_half[:, :, 1])
    theirs_bits = jnp.where(core == 0, by_half[:, :, 1], by_half[:, :, 0])
    bits = jnp.stack([mine_bits, theirs_bits], axis=1)
    bits = jnp.broadcast_to(bits[:, None, :, :, None], (q_blocks, QB, 2, blk_count, half // QB * QB))
    bits = bits.reshape(tok_rows, all_tokens) == 1
    allowed = bits & (key_pos[None, :] <= query_pos[:, None])
    bias = jnp.where(allowed, 0.0, NEG_FILL).astype(jnp.float32)

    q_nope = jnp.transpose(queries[:, :, :DN], (1, 0, 2))
    q_rot = jnp.transpose(queries[:, :, DN:], (1, 0, 2))
    outputs = attention(q_nope, q_rot, expanded, rope_all, bias)
    partial_sum = jnp.dot(outputs, out_weight, preferred_element_type=jnp.float32).astype(jnp.bfloat16)

    pieces = partial_sum.reshape(tok_rows, chips, 2, -1)
    pieces = lax.all_to_all(pieces, "hc", 2, 2, tiled=False)
    paired = pieces.astype(jnp.float32).sum(axis=2).astype(jnp.bfloat16)
    paired = lax.all_to_all(paired, "hh", 1, 1, tiled=False)
    return paired.astype(jnp.float32).sum(axis=1).astype(jnp.bfloat16)


def solution(mesh):
    blk, heads = mesh.devices.shape
    split = Mesh(np.asarray(mesh.devices).reshape(blk, heads // 2, 2), ("blk",) + HEAD)
    return jax.shard_map(
        per_device,
        mesh=split,
        in_specs=(
            P("blk", HEAD),
            P("blk", None),
            P("blk", None),
            P("blk", HEAD),
            P(HEAD, None),
            P(),
        ),
        out_specs=P("blk", HEAD),
        check_vma=False,
    )
```

```python
import math

import jax
import jax.numpy as jnp
import numpy as np
from jax import lax
from jax.experimental import pallas as pl
from jax.experimental.pallas import tpu as pltpu
from jax.sharding import Mesh, PartitionSpec as P

DN = 128
DR = 64
DV = 128
QB = 96


NEG_FILL = -1e30
HEAD = ("hh", "hc")


def attn_kernel(scale, qn_ref, qr_ref, kv_ref, rope_ref, bias_ref, o_ref):
    nt = (((1,), (1,)), ((), ()))
    for j in range(qn_ref.shape[0]):
        base = j * (DN + DV)
        s = lax.dot_general(qn_ref[j], kv_ref[:, base:base + DN], nt, preferred_element_type=jnp.float32)
        s = s + lax.dot_general(qr_ref[j], rope_ref[...], nt, preferred_element_type=jnp.float32)
        s = s * scale + bias_ref[...]
        m = jnp.max(s, axis=1, keepdims=True)
        p = jnp.exp(s - m)
        l = jnp.sum(p, axis=1, keepdims=True)
        o = jnp.dot(p.astype(jnp.bfloat16), kv_ref[:, base + DN:base + DN + DV], preferred_element_type=jnp.float32)
        o_ref[:, j * DV:(j + 1) * DV] = (o / l).astype(o_ref.dtype)


def attention(q_nope, q_rot, expanded, rope_all, bias, per_step=2):
    heads, tok, _ = q_nope.shape
    keys = expanded.shape[0]
    scale = 1.0 / math.sqrt(DN + DR)
    return pl.pallas_call(
        lambda *r: attn_kernel(scale, *r),
        grid=(heads // per_step,),
        in_specs=[
            pl.BlockSpec((per_step, tok, DN), lambda h: (h, 0, 0)),
            pl.BlockSpec((per_step, tok, DR), lambda h: (h, 0, 0)),
            pl.BlockSpec((keys, per_step * (DN + DV)), lambda h: (0, h)),
            pl.BlockSpec((keys, DR), lambda h: (0, 0)),
            pl.BlockSpec((tok, keys), lambda h: (0, 0)),
        ],
        out_specs=pl.BlockSpec((tok, per_step * DV), lambda h: (0, h)),
        out_shape=jax.ShapeDtypeStruct((tok, heads * DV), jnp.bfloat16),
        compiler_params=pltpu.CompilerParams(dimension_semantics=("arbitrary",)),
        cost_estimate=pl.CostEstimate(
            flops=2 * heads * tok * keys * (DN + DR + DV),
            transcendentals=heads * tok * keys,
            bytes_accessed=2 * (expanded.size + heads * tok * (DN + DR + DV) + rope_all.size) + 4 * bias.size,
        ),
    )(q_nope, q_rot, expanded, rope_all, bias)


def per_device(query_heads, latent_cache, rope_keys, up_weight, out_weight, block_mask):
    tok_rows = query_heads.shape[0]
    head_count = out_weight.shape[0] // DV
    blk_count = lax.axis_size("blk")
    chips = lax.axis_size("hh")
    my_index = lax.axis_index("blk")
    core = lax.axis_index("hc")
    all_tokens = tok_rows * blk_count
    half = tok_rows // 2
    kvr = latent_cache.shape[1]
    queries = query_heads.reshape(tok_rows, head_count, DN + DR)

    full_up = lax.all_gather(up_weight, "blk", axis=0, tiled=True)

    payload = jnp.concatenate([latent_cache, rope_keys], axis=1)
    mine = lax.dynamic_slice_in_dim(payload, core * half, half, 0)
    spread = jnp.broadcast_to(mine[None], (blk_count,) + mine.shape)
    mine_all = lax.all_to_all(spread, "blk", 0, 0, tiled=False).reshape(blk_count * half, -1)
    theirs_all = lax.ppermute(mine_all, "hc", [(0, 1), (1, 0)])
    payload_all = jnp.concatenate([mine_all, theirs_all], axis=0)
    latent_all = payload_all[:, :kvr]
    rope_all = payload_all[:, kvr:]

    expanded = jnp.dot(latent_all, full_up, preferred_element_type=jnp.float32).astype(jnp.bfloat16)

    row = jnp.arange(blk_count * half, dtype=jnp.int32)
    block_start = (row // half) * tok_rows + row % half
    key_pos = jnp.concatenate([block_start + core * half, block_start + (1 - core) * half])
    query_pos = my_index * tok_rows + jnp.arange(tok_rows, dtype=jnp.int32)
    q_blocks = tok_rows // QB
    mask_rows = lax.dynamic_slice_in_dim(block_mask, my_index * q_blocks, q_blocks, 0)
    by_half = mask_rows.reshape(q_blocks, blk_count, 2)
    mine_bits = jnp.where(core == 0, by_half[:, :, 0], by_half[:, :, 1])
    theirs_bits = jnp.where(core == 0, by_half[:, :, 1], by_half[:, :, 0])
    bits = jnp.stack([mine_bits, theirs_bits], axis=1)
    bits = jnp.broadcast_to(bits[:, None, :, :, None], (q_blocks, QB, 2, blk_count, half // QB * QB))
    bits = bits.reshape(tok_rows, all_tokens) == 1
    allowed = bits & (key_pos[None, :] <= query_pos[:, None])
    bias = jnp.where(allowed, 0.0, NEG_FILL).astype(jnp.float32)

    q_nope = jnp.transpose(queries[:, :, :DN], (1, 0, 2))
    q_rot = jnp.transpose(queries[:, :, DN:], (1, 0, 2))
    outputs = attention(q_nope, q_rot, expanded, rope_all, bias)
    partial_sum = jnp.dot(outputs, out_weight, preferred_element_type=jnp.float32).astype(jnp.bfloat16)

    pieces = partial_sum.reshape(tok_rows, chips, 2, -1)
    pieces = lax.all_to_all(pieces, "hc", 2, 2, tiled=False)
    paired = pieces.astype(jnp.float32).sum(axis=2).astype(jnp.bfloat16)
    paired = lax.all_to_all(paired, "hh", 1, 1, tiled=False)
    return paired.astype(jnp.float32).sum(axis=1).astype(jnp.bfloat16)


def solution(mesh):
    blk, heads = mesh.devices.shape
    split = Mesh(np.asarray(mesh.devices).reshape(blk, heads // 2, 2), ("blk",) + HEAD)
    return jax.shard_map(
        per_device,
        mesh=split,
        in_specs=(
            P("blk", HEAD),
            P("blk", None),
            P("blk", None),
            P("blk", HEAD),
            P(HEAD, None),
            P(),
        ),
        out_specs=P("blk", HEAD),
        check_vma=False,
    )
```

```python
import math

import jax
import jax.numpy as jnp
import numpy as np
from jax import lax
from jax.experimental import pallas as pl
from jax.experimental.pallas import tpu as pltpu
from jax.sharding import Mesh, PartitionSpec as P

DN = 128
DR = 64
DV = 128
QB = 96


NEG_FILL = -1e30
HEAD = ("hh", "hc")


def attn_kernel(scale, qn_ref, qr_ref, kv_ref, rope_ref, bias_ref, o_ref):
    nt = (((1,), (1,)), ((), ()))
    for j in range(qn_ref.shape[0]):
        base = j * (DN + DV)
        s = lax.dot_general(qn_ref[j], kv_ref[:, base:base + DN], nt, preferred_element_type=jnp.float32)
        s = s + lax.dot_general(qr_ref[j], rope_ref[...], nt, preferred_element_type=jnp.float32)
        s = s * scale + bias_ref[...]
        m = jnp.max(s, axis=1, keepdims=True)
        p = jnp.exp(s - m)
        l = jnp.sum(p, axis=1, keepdims=True)
        o = jnp.dot(p.astype(jnp.bfloat16), kv_ref[:, base + DN:base + DN + DV], preferred_element_type=jnp.float32)
        o_ref[:, j * DV:(j + 1) * DV] = (o / l).astype(o_ref.dtype)


def attention(q_nope, q_rot, expanded, rope_all, bias, per_step=4):
    heads, tok, _ = q_nope.shape
    keys = expanded.shape[0]
    scale = 1.0 / math.sqrt(DN + DR)
    return pl.pallas_call(
        lambda *r: attn_kernel(scale, *r),
        grid=(heads // per_step,),
        in_specs=[
            pl.BlockSpec((per_step, tok, DN), lambda h: (h, 0, 0)),
            pl.BlockSpec((per_step, tok, DR), lambda h: (h, 0, 0)),
            pl.BlockSpec((keys, per_step * (DN + DV)), lambda h: (0, h)),
            pl.BlockSpec((keys, DR), lambda h: (0, 0)),
            pl.BlockSpec((tok, keys), lambda h: (0, 0)),
        ],
        out_specs=pl.BlockSpec((tok, per_step * DV), lambda h: (0, h)),
        out_shape=jax.ShapeDtypeStruct((tok, heads * DV), jnp.bfloat16),
        compiler_params=pltpu.CompilerParams(dimension_semantics=("arbitrary",)),
        cost_estimate=pl.CostEstimate(
            flops=2 * heads * tok * keys * (DN + DR + DV),
            transcendentals=heads * tok * keys,
            bytes_accessed=2 * (expanded.size + heads * tok * (DN + DR + DV) + rope_all.size) + 4 * bias.size,
        ),
    )(q_nope, q_rot, expanded, rope_all, bias)


def per_device(query_heads, latent_cache, rope_keys, up_weight, out_weight, block_mask):
    tok_rows = query_heads.shape[0]
    head_count = out_weight.shape[0] // DV
    blk_count = lax.axis_size("blk")
    chips = lax.axis_size("hh")
    my_index = lax.axis_index("blk")
    core = lax.axis_index("hc")
    all_tokens = tok_rows * blk_count
    half = tok_rows // 2
    kvr = latent_cache.shape[1]
    queries = query_heads.reshape(tok_rows, head_count, DN + DR)

    full_up = lax.all_gather(up_weight, "blk", axis=0, tiled=True)

    payload = jnp.concatenate([latent_cache, rope_keys], axis=1)
    mine = lax.dynamic_slice_in_dim(payload, core * half, half, 0)
    spread = jnp.broadcast_to(mine[None], (blk_count,) + mine.shape)
    mine_all = lax.all_to_all(spread, "blk", 0, 0, tiled=False).reshape(blk_count * half, -1)
    theirs_all = lax.ppermute(mine_all, "hc", [(0, 1), (1, 0)])
    payload_all = jnp.concatenate([mine_all, theirs_all], axis=0)
    latent_all = payload_all[:, :kvr]
    rope_all = payload_all[:, kvr:]

    expanded = jnp.dot(latent_all, full_up, preferred_element_type=jnp.float32).astype(jnp.bfloat16)

    row = jnp.arange(blk_count * half, dtype=jnp.int32)
    block_start = (row // half) * tok_rows + row % half
    key_pos = jnp.concatenate([block_start + core * half, block_start + (1 - core) * half])
    query_pos = my_index * tok_rows + jnp.arange(tok_rows, dtype=jnp.int32)
    q_blocks = tok_rows // QB
    mask_rows = lax.dynamic_slice_in_dim(block_mask, my_index * q_blocks, q_blocks, 0)
    by_half = mask_rows.reshape(q_blocks, blk_count, 2)
    mine_bits = jnp.where(core == 0, by_half[:, :, 0], by_half[:, :, 1])
    theirs_bits = jnp.where(core == 0, by_half[:, :, 1], by_half[:, :, 0])
    bits = jnp.stack([mine_bits, theirs_bits], axis=1)
    bits = jnp.broadcast_to(bits[:, None, :, :, None], (q_blocks, QB, 2, blk_count, half // QB * QB))
    bits = bits.reshape(tok_rows, all_tokens) == 1
    allowed = bits & (key_pos[None, :] <= query_pos[:, None])
    bias = jnp.where(allowed, 0.0, NEG_FILL).astype(jnp.float32)

    q_nope = jnp.transpose(queries[:, :, :DN], (1, 0, 2))
    q_rot = jnp.transpose(queries[:, :, DN:], (1, 0, 2))
    outputs = attention(q_nope, q_rot, expanded, rope_all, bias)
    partial_sum = jnp.dot(outputs, out_weight, preferred_element_type=jnp.float32).astype(jnp.bfloat16)

    pieces = partial_sum.reshape(tok_rows, chips, 2, -1)
    pieces = lax.all_to_all(pieces, "hc", 2, 2, tiled=False)
    paired = pieces.astype(jnp.float32).sum(axis=2).astype(jnp.bfloat16)
    paired = lax.all_to_all(paired, "hh", 1, 1, tiled=False)
    return paired.astype(jnp.float32).sum(axis=1).astype(jnp.bfloat16)


def solution(mesh):
    blk, heads = mesh.devices.shape
    split = Mesh(np.asarray(mesh.devices).reshape(blk, heads // 2, 2), ("blk",) + HEAD)
    return jax.shard_map(
        per_device,
        mesh=split,
        in_specs=(
            P("blk", HEAD),
            P("blk", None),
            P("blk", None),
            P("blk", HEAD),
            P(HEAD, None),
            P(),
        ),
        out_specs=P("blk", HEAD),
        check_vma=False,
    )
```
